256 devices in a mesh: neuron: 32 (over y, z), tm: 2 (over core), trial: 4 (over x).
Axes of the slice: x: 4, y: 4, z: 8, core: 2. Of those that a mesh axis runs over, the one named last changes fastest.
Arguments:
- tensor: bfloat16 [8192, 256, 512], P('neuron', 'tm', 'trial'), may hold values from -6 to 6
- present_blocks: int32 [64, 16], P('neuron'), may hold values 0 or 1
- trial_day: int32 [512], P('trial'), may hold values from 0 to 15
- time_factor: bfloat16 [256, 256], P('tm'), may hold values from 0 to 1
- trial_factor: bfloat16 [512, 256], P('trial'), may hold values from 0 to 1
Outputs:
- neuron_out: bfloat16 [8192, 256], P(('neuron', 'tm', 'trial'))
- time_out: bfloat16 [256, 256], P('tm')
- trial_out: bfloat16 [512, 256], P('trial')
The draws below stay inside these ranges and needn't reach their ends.
All inputs are finite; a program needn't handle non-finite values. No bound on the sum of `present_blocks` on one device may be relied on, other than what follows from the above.
Results may differ from the reference program's by a relative error of at most 0.0051.
The reference program's roundings to bfloat16 on the way count: a program that leaves them out, or rounds other values in their place, can miss the bound.
Values may be sent and summed in bfloat16 or wider, within the bound.
No kernel may reach another device: no remote copies, remote signals or barrier semaphores. Data moves between devices by JAX's collectives and lax.ppermute only.
A program may use at most 128 MiB of HBM per device.

```python
import jax
import jax.numpy as jnp
from jax import lax

R = 256
BLOCK = 128
DAYS = 16
NBLK = 64
NEU = 8192
TIME = 256
TRIALS = 512


def touch_ends(entries, own_key, smallest, largest):
    longest = entries.shape.index(max(entries.shape))
    spots = []
    for shift in (0, 1):
        where = [jax.random.randint(jax.random.fold_in(own_key, axis), (), 0, length) for axis, length in enumerate(entries.shape)]
        where[longest] = (where[longest] + shift) % entries.shape[longest]
        spots.append(tuple(where))
    return entries.at[spots[0]].set(smallest).at[spots[1]].set(largest)


def with_spikes(drawn, own_key, source, target, parts, factor):
    def block_of(dim):
        return (jnp.arange(drawn.shape[dim]) // (drawn.shape[dim] // parts)).reshape((-1,) + (1,) * (drawn.ndim - 1 - dim))

    near = jax.random.permutation(own_key, parts)[block_of(target)]
    second = (block_of(target) + parts // 2) % parts
    return jnp.where((block_of(source) == near) | (block_of(source) == second), factor * drawn, drawn)


def levels(own_key, shape, pieces, low, largest):
    def one(position, parts):
        steps = jax.random.uniform(jax.random.fold_in(jax.random.fold_in(own_key, 6), position), (parts,), jnp.float32, low / len(pieces), largest / len(pieces))
        return jnp.repeat(jnp.exp(steps), shape[position] // parts).reshape((-1,) + (1,) * (len(shape) - position - 1))

    factor_of = one(*pieces[0])
    for cut in pieces[1:]:
        factor_of = factor_of * one(*cut)
    return factor_of


def gaussian_with(rng, dims, width, bound, split, heavy, kind=jnp.bfloat16):
    drawn = width * jax.random.normal(rng, dims, jnp.float32)
    if split:
        drawn = drawn * levels(rng, dims, split, -0.22, 0.18)
    return jnp.clip(with_spikes(drawn, jax.random.fold_in(rng, 3), *heavy), -bound, bound).astype(kind)


def setup_inputs(seed: int = 0) -> dict:
    key_of = jax.random.split(jax.random.key(seed), 6)
    return {
        "tensor": gaussian_with(key_of[0], (NEU, TIME, TRIALS), 1.0, 6.0, ((0, 32), (1, 2), (2, 4)), (0, 1, 32, 2.75)),
        "present_blocks": touch_ends((jax.random.randint(key_of[1], (NBLK, DAYS), 0, 4) < 3).astype(jnp.int32), jax.random.fold_in(key_of[1], 1), 0, 1),
        "trial_day": touch_ends(jax.random.randint(key_of[2], (TRIALS,), 0, DAYS), jax.random.fold_in(key_of[2], 1), 0, DAYS - 1).astype(jnp.int32),
        "time_factor": jnp.clip(1.0 * jax.random.uniform(key_of[3], (TIME, R), jnp.float32) ** levels(key_of[3], (TIME, R), ((0, 2),), -0.2, 0.2), 0.0, 1.0).astype(jnp.bfloat16),
        "trial_factor": jnp.clip(1.0 * jax.random.uniform(key_of[4], (TRIALS, R), jnp.float32) ** levels(key_of[4], (TRIALS, R), ((0, 4),), -0.2, 0.2), 0.0, 1.0).astype(jnp.bfloat16),
    }


RIDGE = 0.1
EPSILON = 1e-06

def normal_inverse(gram_matrix):
    order_size = gram_matrix.shape[0]
    identity = jnp.eye(order_size, dtype=jnp.float32)
    scaled = gram_matrix / jnp.mean(jnp.diagonal(gram_matrix)) + RIDGE * identity
    lower_factor = jnp.linalg.cholesky(scaled)
    return jax.scipy.linalg.cho_solve((lower_factor, True), identity)

def khatri_rao(left_rows, right_rows):
    return (left_rows.astype(jnp.float32)[:, None, :] * right_rows.astype(jnp.float32)[None, :, :]).astype(jnp.bfloat16)

def rescale(raw_rows, total_rows):
    gram_raw = jnp.dot(raw_rows.T, raw_rows, precision=lax.Precision.HIGHEST)
    scales = jnp.sqrt(jnp.diagonal(gram_raw) / total_rows + EPSILON)
    factor = (raw_rows / scales[None, :]).astype(jnp.bfloat16)
    normed = gram_raw / (scales[:, None] * scales[None, :])
    return (factor, normed)

def reference(tensor, present_blocks, trial_day, time_factor, trial_factor):
    block_mask = present_blocks[:, trial_day].astype(jnp.float32)
    tensor_blocks = tensor.reshape(NBLK, BLOCK, TIME, TRIALS)
    gram_time = jnp.dot(time_factor.T.astype(jnp.float32), time_factor.astype(jnp.float32), preferred_element_type=jnp.float32)
    gram_trial = jnp.dot(trial_factor.T.astype(jnp.float32), trial_factor.astype(jnp.float32), preferred_element_type=jnp.float32)
    kr_tk = khatri_rao(time_factor, trial_factor).astype(jnp.float32)

    def neuron_block(inputs):
        tensor_piece, mask_row = inputs
        masked = tensor_piece.astype(jnp.float32) * mask_row[None, None, :]
        return jnp.einsum('itk,tkr->ir', masked, kr_tk, precision=lax.Precision.HIGHEST)
    mttkrp_neuron = lax.map(neuron_block, (tensor_blocks, block_mask)).reshape(NEU, R)
    raw_neuron = jnp.dot(mttkrp_neuron, normal_inverse(gram_time * gram_trial), precision=lax.Precision.HIGHEST)
    neuron_out, gram_neuron = rescale(raw_neuron, NEU)
    neuron_blocks = neuron_out.reshape(NBLK, BLOCK, R)

    def time_block(running, inputs):
        tensor_piece, mask_row, rows_a = inputs
        masked = tensor_piece.astype(jnp.float32) * mask_row[None, None, :]
        kr_ik = khatri_rao(rows_a, trial_factor).astype(jnp.float32)
        return (running + jnp.einsum('itk,ikr->tr', masked, kr_ik, precision=lax.Precision.HIGHEST), None)
    mttkrp_time, unused = lax.scan(time_block, jnp.zeros((TIME, R), jnp.float32), (tensor_blocks, block_mask, neuron_blocks))
    raw_time = jnp.dot(mttkrp_time, normal_inverse(gram_neuron * gram_trial), precision=lax.Precision.HIGHEST)
    time_out, gram_time_new = rescale(raw_time, TIME)

    def trial_block(running, inputs):
        tensor_piece, mask_row, rows_a = inputs
        masked = tensor_piece.astype(jnp.float32) * mask_row[None, None, :]
        kr_it = khatri_rao(rows_a, time_out).astype(jnp.float32)
        return (running + jnp.einsum('itk,itr->kr', masked, kr_it, precision=lax.Precision.HIGHEST), None)
    mttkrp_trial, unused = lax.scan(trial_block, jnp.zeros((TRIALS, R), jnp.float32), (tensor_blocks, block_mask, neuron_blocks))
    raw_trial = jnp.dot(mttkrp_trial, normal_inverse(gram_neuron * gram_time_new), precision=lax.Precision.HIGHEST)
    scales = jnp.sqrt(lax.optimization_barrier(jnp.sum(raw_trial * raw_trial, axis=0)) / TRIALS + EPSILON)
    trial_out = (raw_trial / scales[None, :]).astype(jnp.bfloat16)
    return (neuron_out, time_out, trial_out)
```

```python
import jax
import jax.numpy as jnp
from jax import lax
from jax.sharding import PartitionSpec as P

RIDGE = 0.1
EPSILON = 1e-06


def normal_inverse(gram_matrix):
    order_size = gram_matrix.shape[0]
    identity = jnp.eye(order_size, dtype=jnp.float32)
    scaled = gram_matrix / jnp.mean(jnp.diagonal(gram_matrix)) + RIDGE * identity
    lower_factor = jnp.linalg.cholesky(scaled)
    return jax.scipy.linalg.cho_solve((lower_factor, True), identity)


def apply_inverse(partial_sums, inverse):
    return jnp.dot(partial_sums, inverse, precision=lax.Precision.HIGHEST)


def raw_gram(raw_rows):
    return jnp.dot(raw_rows.T, raw_rows, precision=lax.Precision.HIGHEST)


def khatri_rao(left_rows, right_rows):
    return (
        left_rows.astype(jnp.float32)[:, None, :] * right_rows.astype(jnp.float32)[None, :, :]
    ).astype(jnp.bfloat16)


def rescale(raw_rows, gram_sum, total_rows):
    scales = jnp.sqrt(jnp.diagonal(gram_sum) / total_rows + EPSILON)
    factor = (raw_rows / scales[None, :]).astype(jnp.bfloat16)
    normed = gram_sum / (scales[:, None] * scales[None, :])
    return (factor, normed)


def mask_tensor(tensor, present_blocks, trial_day):
    day_count = present_blocks.shape[1]
    onehot = (trial_day[:, None] == jnp.arange(day_count, dtype=jnp.int32)[None, :]).astype(
        jnp.float32
    )
    block_mask = jnp.dot(present_blocks.astype(jnp.float32), onehot.T)
    block_count = present_blocks.shape[0]
    shaped = tensor.reshape(
        block_count, tensor.shape[0] // block_count, tensor.shape[1], tensor.shape[2]
    )
    return shaped * block_mask.astype(jnp.bfloat16)[:, None, None, :]


def factor_gram(rows):
    return jnp.dot(rows.T, rows, preferred_element_type=jnp.float32)


def on_device(tensor, present_blocks, trial_day, time_factor, trial_factor):
    time_all = lax.all_gather(time_factor, "tm", axis=0, tiled=True)
    trial_all = lax.all_gather(trial_factor, "trial", axis=0, tiled=True)
    blocks = mask_tensor(tensor, present_blocks, trial_day)
    block_count, block_rows, time_rows, trial_rows = blocks.shape
    neuron_rows = block_count * block_rows
    flattened = blocks.reshape(neuron_rows, time_rows, trial_rows)
    rank_size = time_factor.shape[1]
    start_time = factor_gram(time_all)
    start_trial = factor_gram(trial_all)
    inverse_neuron = normal_inverse(start_time * start_trial)
    kr_tk = khatri_rao(time_factor, trial_factor)
    neuron_total = neuron_rows * lax.axis_size("neuron")
    block_sums = lax.psum(
        jnp.einsum("itk,tkr->ir", flattened, kr_tk, preferred_element_type=jnp.float32),
        ("tm", "trial"),
    )
    raw_rows = apply_inverse(block_sums, inverse_neuron)
    gram_sum = lax.psum(raw_gram(raw_rows), "neuron")
    neuron_local, gram_neuron = rescale(raw_rows, gram_sum, neuron_total)
    own_rows = neuron_rows // (lax.axis_size("tm") * lax.axis_size("trial"))
    own_index = lax.axis_index("tm") * lax.axis_size("trial") + lax.axis_index("trial")
    neuron_own = lax.dynamic_slice_in_dim(neuron_local, own_index * own_rows, own_rows, axis=0)
    neuron_blocks = neuron_local.reshape(block_count, block_rows, rank_size)
    time_total = time_rows * lax.axis_size("tm")
    inverse_time = normal_inverse(gram_neuron * start_trial)

    def time_add_block(running, inputs):
        tensor_piece, rows_a = inputs
        kr_ik = khatri_rao(rows_a, trial_factor)
        return (
            running
            + jnp.einsum("itk,ikr->tr", tensor_piece, kr_ik, preferred_element_type=jnp.float32),
            None,
        )

    running, unused = lax.scan(
        time_add_block,
        jnp.zeros((time_rows, rank_size), jnp.float32),
        (blocks, neuron_blocks),
    )
    half_sums = lax.psum(running, ("neuron", "trial"))
    raw_rows = apply_inverse(half_sums, inverse_time)
    gram_sum = lax.psum(raw_gram(raw_rows), "tm")
    time_local, gram_time = rescale(raw_rows, gram_sum, time_total)
    trial_total = trial_rows * lax.axis_size("trial")
    inverse_trial = normal_inverse(gram_neuron * gram_time)

    def trial_add_block(running, inputs):
        tensor_piece, rows_a = inputs
        kr_it = khatri_rao(rows_a, time_local)
        return (
            running
            + jnp.einsum("itk,itr->kr", tensor_piece, kr_it, preferred_element_type=jnp.float32),
            None,
        )

    running, unused = lax.scan(
        trial_add_block,
        jnp.zeros((trial_rows, rank_size), jnp.float32),
        (blocks, neuron_blocks),
    )
    quarter_sums = lax.psum(running, ("neuron", "tm"))
    raw_rows = apply_inverse(quarter_sums, inverse_trial)
    squares = lax.psum(jnp.sum(raw_rows * raw_rows, axis=0), "trial")
    scales = jnp.sqrt(squares / trial_total + EPSILON)
    trial_local = (raw_rows / scales[None, :]).astype(jnp.bfloat16)
    return (neuron_own, time_local, trial_local)


def solution(mesh):
    return jax.shard_map(
        on_device,
        mesh=mesh,
        in_specs=(
            P("neuron", "tm", "trial"),
            P("neuron", None),
            P("trial"),
            P("tm", None),
            P("trial", None),
        ),
        out_specs=(P(("neuron", "tm", "trial"), None), P("tm", None), P("trial", None)),
        check_vma=False,
    )
```

```python
import jax
import jax.numpy as jnp
from jax import lax
from jax.sharding import PartitionSpec as P

RIDGE = 0.1
EPSILON = 1e-06


def normal_inverse(gram_matrix):
    order_size = gram_matrix.shape[0]
    identity = jnp.eye(order_size, dtype=jnp.float32)
    scaled = gram_matrix / jnp.mean(jnp.diagonal(gram_matrix)) + RIDGE * identity
    lower_factor = jnp.linalg.cholesky(scaled)
    return jax.scipy.linalg.cho_solve((lower_factor, True), identity)


def apply_inverse(partial_sums, inverse):
    return jnp.dot(partial_sums, inverse, precision=lax.Precision.HIGHEST)


def raw_gram(raw_rows):
    return jnp.dot(raw_rows.T, raw_rows, precision=lax.Precision.HIGHEST)


def khatri_rao(left_rows, right_rows):
    return (
        left_rows.astype(jnp.float32)[:, None, :] * right_rows.astype(jnp.float32)[None, :, :]
    ).astype(jnp.bfloat16)


def rescale(raw_rows, gram_sum, total_rows):
    scales = jnp.sqrt(jnp.diagonal(gram_sum) / total_rows + EPSILON)
    factor = (raw_rows / scales[None, :]).astype(jnp.bfloat16)
    normed = gram_sum / (scales[:, None] * scales[None, :])
    return (factor, normed)


def mask_tensor(tensor, present_blocks, trial_day):
    day_count = present_blocks.shape[1]
    onehot = (trial_day[:, None] == jnp.arange(day_count, dtype=jnp.int32)[None, :]).astype(
        jnp.float32
    )
    block_mask = jnp.dot(present_blocks.astype(jnp.float32), onehot.T)
    block_count = present_blocks.shape[0]
    shaped = tensor.reshape(
        block_count, tensor.shape[0] // block_count, tensor.shape[1], tensor.shape[2]
    )
    return shaped * block_mask.astype(jnp.bfloat16)[:, None, None, :]


def tree_sum(values, axes):
    for axis in axes:
        size = lax.axis_size(axis)
        stride = 1
        while stride < size:
            pairs = [(i, i ^ stride) for i in range(size)]
            values = values + lax.ppermute(values, axis, pairs)
            stride *= 2
    return values


def factor_gram(rows):
    return jnp.dot(rows.T, rows, preferred_element_type=jnp.float32)


def on_device(tensor, present_blocks, trial_day, time_factor, trial_factor):
    blocks = mask_tensor(tensor, present_blocks, trial_day)
    block_count, block_rows, time_rows, trial_rows = blocks.shape
    neuron_rows = block_count * block_rows
    flattened = blocks.reshape(neuron_rows, time_rows, trial_rows)
    rank_size = time_factor.shape[1]
    start_time = tree_sum(factor_gram(time_factor), ("tm",))
    start_trial = tree_sum(factor_gram(trial_factor), ("trial",))
    inverse_neuron = normal_inverse(start_time * start_trial)
    kr_tk = khatri_rao(time_factor, trial_factor)
    neuron_total = neuron_rows * lax.axis_size("neuron")
    block_sums = tree_sum(
        jnp.einsum("itk,tkr->ir", flattened, kr_tk, preferred_element_type=jnp.float32),
        ("tm", "trial"),
    )
    raw_rows = apply_inverse(block_sums, inverse_neuron)
    gram_sum = tree_sum(raw_gram(raw_rows), ("neuron",))
    neuron_local, gram_neuron = rescale(raw_rows, gram_sum, neuron_total)
    own_rows = neuron_rows // (lax.axis_size("tm") * lax.axis_size("trial"))
    own_index = lax.axis_index("tm") * lax.axis_size("trial") + lax.axis_index("trial")
    neuron_own = lax.dynamic_slice_in_dim(neuron_local, own_index * own_rows, own_rows, axis=0)
    neuron_blocks = neuron_local.reshape(block_count, block_rows, rank_size)
    time_total = time_rows * lax.axis_size("tm")

    def time_add_block(running, inputs):
        tensor_piece, rows_a = inputs
        kr_ik = khatri_rao(rows_a, trial_factor)
        return (
            running
            + jnp.einsum("itk,ikr->tr", tensor_piece, kr_ik, preferred_element_type=jnp.float32),
            None,
        )

    running, unused = lax.scan(
        time_add_block,
        jnp.zeros((time_rows, rank_size), jnp.float32),
        (blocks, neuron_blocks),
    )
    running, gram_neuron = lax.optimization_barrier((running, gram_neuron))
    half_sums = tree_sum(running, ("neuron", "trial"))
    inverse_time = normal_inverse(gram_neuron * start_trial)
    raw_rows = apply_inverse(half_sums, inverse_time)
    gram_sum = tree_sum(raw_gram(raw_rows), ("tm",))
    time_local, gram_time = rescale(raw_rows, gram_sum, time_total)
    trial_total = trial_rows * lax.axis_size("trial")

    def trial_add_block(running, inputs):
        tensor_piece, rows_a = inputs
        kr_it = khatri_rao(rows_a, time_local)
        return (
            running
            + jnp.einsum("itk,itr->kr", tensor_piece, kr_it, preferred_element_type=jnp.float32),
            None,
        )

    running, unused = lax.scan(
        trial_add_block,
        jnp.zeros((trial_rows, rank_size), jnp.float32),
        (blocks, neuron_blocks),
    )
    running, gram_time = lax.optimization_barrier((running, gram_time))
    quarter_sums = tree_sum(running, ("neuron", "tm"))
    inverse_trial = normal_inverse(gram_neuron * gram_time)
    raw_rows = apply_inverse(quarter_sums, inverse_trial)
    squares = tree_sum(jnp.sum(raw_rows * raw_rows, axis=0), ("trial",))
    scales = jnp.sqrt(squares / trial_total + EPSILON)
    trial_local = (raw_rows / scales[None, :]).astype(jnp.bfloat16)
    return (neuron_own, time_local, trial_local)


def solution(mesh):
    return jax.shard_map(
        on_device,
        mesh=mesh,
        in_specs=(
            P("neuron", "tm", "trial"),
            P("neuron", None),
            P("trial"),
            P("tm", None),
            P("trial", None),
        ),
        out_specs=(P(("neuron", "tm", "trial"), None), P("tm", None), P("trial", None)),
        check_vma=False,
    )
```

```python
import jax
import jax.numpy as jnp
from jax import lax
from jax.sharding import PartitionSpec as P

RIDGE = 0.1
EPSILON = 1e-06


def normal_inverse(gram_matrix):
    order_size = gram_matrix.shape[0]
    identity = jnp.eye(order_size, dtype=jnp.float32)
    scaled = gram_matrix / jnp.mean(jnp.diagonal(gram_matrix)) + RIDGE * identity
    lower_factor = jnp.linalg.cholesky(scaled)
    return lax.linalg.triangular_solve(lower_factor, identity, left_side=True, lower=True)


def apply_inverse(partial_sums, inverse_factor):
    half = jnp.dot(partial_sums, inverse_factor.T, precision=lax.Precision.HIGHEST)
    return jnp.dot(half, inverse_factor, precision=lax.Precision.HIGHEST)


def raw_gram(raw_rows):
    return jnp.dot(raw_rows.T, raw_rows, precision=lax.Precision.HIGHEST)


def khatri_rao(left_rows, right_rows):
    return (
        left_rows.astype(jnp.float32)[:, None, :] * right_rows.astype(jnp.float32)[None, :, :]
    ).astype(jnp.bfloat16)


def rescale(raw_rows, gram_sum, total_rows):
    scales = jnp.sqrt(jnp.diagonal(gram_sum) / total_rows + EPSILON)
    factor = (raw_rows / scales[None, :]).astype(jnp.bfloat16)
    normed = gram_sum / (scales[:, None] * scales[None, :])
    return (factor, normed)


def block_mask_of(present_blocks, trial_day):
    day_count = present_blocks.shape[1]
    onehot = (trial_day[:, None] == jnp.arange(day_count, dtype=jnp.int32)[None, :]).astype(
        jnp.float32
    )
    return jnp.dot(present_blocks.astype(jnp.float32), onehot.T).astype(jnp.bfloat16)


def tree_sum(values, axes):
    for axis in axes:
        size = lax.axis_size(axis)
        stride = 1
        while stride < size:
            pairs = [(i, i ^ stride) for i in range(size)]
            values = values + lax.ppermute(values, axis, pairs)
            stride *= 2
    return values


def factor_gram(rows):
    return jnp.dot(rows.T, rows, preferred_element_type=jnp.float32)


def on_device(tensor, present_blocks, trial_day, time_factor, trial_factor):
    block_mask = block_mask_of(present_blocks, trial_day)
    block_count = present_blocks.shape[0]
    neuron_rows, time_rows, trial_rows = tensor.shape
    block_rows = neuron_rows // block_count
    blocks = tensor.reshape(block_count, block_rows, time_rows, trial_rows)
    rank_size = time_factor.shape[1]
    start_time = tree_sum(factor_gram(time_factor), ("tm",))
    start_trial = tree_sum(factor_gram(trial_factor), ("trial",))
    inverse_neuron = normal_inverse(start_time * start_trial)
    kr_tk = khatri_rao(time_factor, trial_factor)
    neuron_total = neuron_rows * lax.axis_size("neuron")
    kr_masked = kr_tk[None, :, :, :] * block_mask[:, None, :, None]
    block_sums = tree_sum(
        jnp.einsum(
            "bitk,btkr->bir", blocks, kr_masked, preferred_element_type=jnp.float32
        ).reshape(neuron_rows, rank_size),
        ("tm", "trial"),
    )
    raw_rows = apply_inverse(block_sums, inverse_neuron)
    gram_sum = tree_sum(raw_gram(raw_rows), ("neuron",))
    neuron_local, gram_neuron = rescale(raw_rows, gram_sum, neuron_total)
    own_rows = neuron_rows // (lax.axis_size("tm") * lax.axis_size("trial"))
    own_index = lax.axis_index("tm") * lax.axis_size("trial") + lax.axis_index("trial")
    neuron_own = lax.dynamic_slice_in_dim(neuron_local, own_index * own_rows, own_rows, axis=0)
    neuron_blocks = neuron_local.reshape(block_count, block_rows, rank_size)
    time_total = time_rows * lax.axis_size("tm")

    def time_add_block(running, inputs):
        tensor_piece, mask_row, rows_a = inputs
        kr_ik = khatri_rao(rows_a, trial_factor) * mask_row[None, :, None]
        return (
            running
            + jnp.einsum("itk,ikr->tr", tensor_piece, kr_ik, preferred_element_type=jnp.float32),
            None,
        )

    running, unused = lax.scan(
        time_add_block,
        jnp.zeros((time_rows, rank_size), jnp.float32),
        (blocks, block_mask, neuron_blocks),
    )
    running, gram_neuron = lax.optimization_barrier((running, gram_neuron))
    half_sums = tree_sum(running, ("neuron", "trial"))
    inverse_time = normal_inverse(gram_neuron * start_trial)
    raw_rows = apply_inverse(half_sums, inverse_time)
    gram_sum = tree_sum(raw_gram(raw_rows), ("tm",))
    time_local, gram_time = rescale(raw_rows, gram_sum, time_total)
    trial_total = trial_rows * lax.axis_size("trial")

    def trial_add_block(running, inputs):
        tensor_piece, mask_row, rows_a = inputs
        kr_it = khatri_rao(rows_a, time_local)
        block_part = jnp.einsum(
            "itk,itr->kr", tensor_piece, kr_it, preferred_element_type=jnp.float32
        )
        return (running + block_part * mask_row.astype(jnp.float32)[:, None], None)

    running, unused = lax.scan(
        trial_add_block,
        jnp.zeros((trial_rows, rank_size), jnp.float32),
        (blocks, block_mask, neuron_blocks),
    )
    running, gram_time = lax.optimization_barrier((running, gram_time))
    quarter_sums = tree_sum(running, ("neuron", "tm"))
    inverse_trial = normal_inverse(gram_neuron * gram_time)
    raw_rows = apply_inverse(quarter_sums, inverse_trial)
    squares = tree_sum(jnp.sum(raw_rows * raw_rows, axis=0), ("trial",))
    scales = jnp.sqrt(squares / trial_total + EPSILON)
    trial_local = (raw_rows / scales[None, :]).astype(jnp.bfloat16)
    return (neuron_own, time_local, trial_local)


def solution(mesh):
    return jax.shard_map(
        on_device,
        mesh=mesh,
        in_specs=(
            P("neuron", "tm", "trial"),
            P("neuron", None),
            P("trial"),
            P("tm", None),
            P("trial", None),
        ),
        out_specs=(P(("neuron", "tm", "trial"), None), P("tm", None), P("trial", None)),
        check_vma=False,
    )
```

```python
import jax
import jax.numpy as jnp
from jax import lax
from jax.sharding import PartitionSpec as P

RIDGE = 0.1
EPSILON = 1e-06


def normal_inverse(gram_matrix):
    order_size = gram_matrix.shape[0]
    identity = jnp.eye(order_size, dtype=jnp.float32)
    scaled = gram_matrix / jnp.mean(jnp.diagonal(gram_matrix)) + RIDGE * identity
    lower_factor = jnp.linalg.cholesky(scaled)
    return lax.linalg.triangular_solve(lower_factor, identity, left_side=True, lower=True)


def apply_inverse(partial_sums, inverse_factor):
    half = jnp.dot(partial_sums, inverse_factor.T, precision=lax.Precision.HIGHEST)
    return jnp.dot(half, inverse_factor, precision=lax.Precision.HIGHEST)


def raw_gram(raw_rows):
    return jnp.dot(raw_rows.T, raw_rows, precision=lax.Precision.HIGHEST)


def khatri_rao(left_rows, right_rows):
    return (
        left_rows.astype(jnp.float32)[:, None, :] * right_rows.astype(jnp.float32)[None, :, :]
    ).astype(jnp.bfloat16)


def rescale(raw_rows, gram_sum, total_rows):
    scales = jnp.sqrt(jnp.diagonal(gram_sum) / total_rows + EPSILON)
    factor = (raw_rows / scales[None, :]).astype(jnp.bfloat16)
    normed = gram_sum / (scales[:, None] * scales[None, :])
    return (factor, normed)


def block_mask_of(present_blocks, trial_day):
    day_count = present_blocks.shape[1]
    onehot = (trial_day[:, None] == jnp.arange(day_count, dtype=jnp.int32)[None, :]).astype(
        jnp.float32
    )
    return jnp.dot(present_blocks.astype(jnp.float32), onehot.T).astype(jnp.bfloat16)


def tree_sum(values, axes):
    for axis in axes:
        size = lax.axis_size(axis)
        stride = 1
        while stride < size:
            pairs = [(i, i ^ stride) for i in range(size)]
            values = values + lax.ppermute(values, axis, pairs)
            stride *= 2
    return values


def factor_gram(rows):
    return jnp.dot(rows.T, rows, preferred_element_type=jnp.float32)


def on_device(tensor, present_blocks, trial_day, time_factor, trial_factor):
    block_mask = block_mask_of(present_blocks, trial_day)
    block_count = present_blocks.shape[0]
    neuron_rows, time_rows, trial_rows = tensor.shape
    block_rows = neuron_rows // block_count
    blocks = tensor.reshape(block_count, block_rows, time_rows, trial_rows)
    rank_size = time_factor.shape[1]
    start_time = tree_sum(factor_gram(time_factor), ("tm",))
    start_trial = tree_sum(factor_gram(trial_factor), ("trial",))
    inverse_neuron = normal_inverse(start_time * start_trial)
    kr_tk = khatri_rao(time_factor, trial_factor)
    neuron_total = neuron_rows * lax.axis_size("neuron")
    kr_masked = (kr_tk[None, :, :, :] * block_mask[:, None, :, None]).reshape(
        block_count, time_rows * trial_rows, rank_size
    )
    block_sums = tree_sum(
        jnp.einsum(
            "bix,bxr->bir",
            tensor.reshape(block_count, block_rows, time_rows * trial_rows),
            kr_masked,
            preferred_element_type=jnp.float32,
        ).reshape(neuron_rows, rank_size),
        ("tm", "trial"),
    )
    raw_rows = apply_inverse(block_sums, inverse_neuron)
    gram_sum = tree_sum(raw_gram(raw_rows), ("neuron",))
    neuron_local, gram_neuron = rescale(raw_rows, gram_sum, neuron_total)
    own_rows = neuron_rows // (lax.axis_size("tm") * lax.axis_size("trial"))
    own_index = lax.axis_index("tm") * lax.axis_size("trial") + lax.axis_index("trial")
    neuron_own = lax.dynamic_slice_in_dim(neuron_local, own_index * own_rows, own_rows, axis=0)
    neuron_blocks = neuron_local.reshape(block_count, block_rows, rank_size)
    time_total = time_rows * lax.axis_size("tm")

    def time_add_block(running, inputs):
        tensor_piece, mask_row, rows_a = inputs
        kr_ik = khatri_rao(rows_a, trial_factor) * mask_row[None, :, None]
        return (
            running
            + jnp.einsum("itk,ikr->tr", tensor_piece, kr_ik, preferred_element_type=jnp.float32),
            None,
        )

    running, unused = lax.scan(
        time_add_block,
        jnp.zeros((time_rows, rank_size), jnp.float32),
        (blocks, block_mask, neuron_blocks),
    )
    running, gram_neuron = lax.optimization_barrier((running, gram_neuron))
    half_sums = tree_sum(running, ("neuron", "trial"))
    inverse_time = normal_inverse(gram_neuron * start_trial)
    raw_rows = apply_inverse(half_sums, inverse_time)
    gram_sum = tree_sum(raw_gram(raw_rows), ("tm",))
    time_local, gram_time = rescale(raw_rows, gram_sum, time_total)
    trial_total = trial_rows * lax.axis_size("trial")

    def trial_add_block(running, inputs):
        tensor_piece, mask_row, rows_a = inputs
        kr_ti = (
            rows_a.T.astype(jnp.float32)[:, :, None] * time_local.T.astype(jnp.float32)[:, None, :]
        ).astype(jnp.bfloat16)
        block_part = jnp.dot(
            kr_ti.reshape(rank_size, block_rows * time_rows),
            tensor_piece.reshape(block_rows * time_rows, trial_rows),
            preferred_element_type=jnp.float32,
        )
        return (running + block_part * mask_row.astype(jnp.float32)[None, :], None)

    running, unused = lax.scan(
        trial_add_block,
        jnp.zeros((rank_size, trial_rows), jnp.float32),
        (blocks, block_mask, neuron_blocks),
    )
    running = running.T
    running, gram_time = lax.optimization_barrier((running, gram_time))
    quarter_sums = tree_sum(running, ("neuron", "tm"))
    inverse_trial = normal_inverse(gram_neuron * gram_time)
    raw_rows = apply_inverse(quarter_sums, inverse_trial)
    squares = tree_sum(jnp.sum(raw_rows * raw_rows, axis=0), ("trial",))
    scales = jnp.sqrt(squares / trial_total + EPSILON)
    trial_local = (raw_rows / scales[None, :]).astype(jnp.bfloat16)
    return (neuron_own, time_local, trial_local)


def solution(mesh):
    return jax.shard_map(
        on_device,
        mesh=mesh,
        in_specs=(
            P("neuron", "tm", "trial"),
            P("neuron", None),
            P("trial"),
            P("tm", None),
            P("trial", None),
        ),
        out_specs=(P(("neuron", "tm", "trial"), None), P("tm", None), P("trial", None)),
        check_vma=False,
    )
```

```python
import jax
import jax.numpy as jnp
from jax import lax
from jax.sharding import PartitionSpec as P

RIDGE = 0.1
EPSILON = 1e-06


def normal_inverse(gram_matrix):
    order_size = gram_matrix.shape[0]
    identity = jnp.eye(order_size, dtype=jnp.float32)
    scaled = gram_matrix / jnp.mean(jnp.diagonal(gram_matrix)) + RIDGE * identity
    lower_factor = jnp.linalg.cholesky(scaled)
    return lax.linalg.triangular_solve(lower_factor, identity, left_side=True, lower=True)


def apply_inverse(partial_sums, inverse_factor):
    half = jnp.dot(partial_sums, inverse_factor.T, precision=lax.Precision.HIGHEST)
    return jnp.dot(half, inverse_factor, precision=lax.Precision.HIGHEST)


def raw_gram(raw_rows):
    return jnp.dot(raw_rows.T, raw_rows, precision=lax.Precision.HIGHEST)


def khatri_rao(left_rows, right_rows):
    return (
        left_rows.astype(jnp.float32)[:, None, :] * right_rows.astype(jnp.float32)[None, :, :]
    ).astype(jnp.bfloat16)


def rescale(raw_rows, gram_sum, total_rows):
    scales = jnp.sqrt(jnp.diagonal(gram_sum) / total_rows + EPSILON)
    factor = (raw_rows / scales[None, :]).astype(jnp.bfloat16)
    normed = gram_sum / (scales[:, None] * scales[None, :])
    return (factor, normed)


def block_mask_of(present_blocks, trial_day):
    day_count = present_blocks.shape[1]
    onehot = (trial_day[:, None] == jnp.arange(day_count, dtype=jnp.int32)[None, :]).astype(
        jnp.float32
    )
    return jnp.dot(present_blocks.astype(jnp.float32), onehot.T).astype(jnp.bfloat16)


def tree_sum(values, axes):
    for axis in axes:
        size = lax.axis_size(axis)
        stride = 1
        while stride < size:
            pairs = [(i, i ^ stride) for i in range(size)]
            values = values + lax.ppermute(values, axis, pairs)
            stride *= 2
    return values


def tree_gather(piece, steps):
    for axis, stride in steps:
        pairs = [(i, i ^ stride) for i in range(lax.axis_size(axis))]
        other = lax.ppermute(piece, axis, pairs)
        upper = (lax.axis_index(axis) // stride) % 2 == 1
        piece = jnp.where(
            upper,
            jnp.concatenate([other, piece], axis=0),
            jnp.concatenate([piece, other], axis=0),
        )
    return piece


def factor_gram(rows):
    return jnp.dot(rows.T, rows, preferred_element_type=jnp.float32)


def on_device(tensor, present_blocks, trial_day, time_factor, trial_factor):
    block_mask = block_mask_of(present_blocks, trial_day)
    block_count = present_blocks.shape[0]
    neuron_rows, time_rows, trial_rows = tensor.shape
    block_rows = neuron_rows // block_count
    blocks = tensor.reshape(block_count, block_rows, time_rows, trial_rows)
    rank_size = time_factor.shape[1]
    start_time = tree_sum(factor_gram(time_factor), ("tm",))
    start_trial = tree_sum(factor_gram(trial_factor), ("trial",))
    inverse_neuron = normal_inverse(start_time * start_trial)
    kr_tk = khatri_rao(time_factor, trial_factor)
    neuron_total = neuron_rows * lax.axis_size("neuron")
    kr_masked = kr_tk[None, :, :, :] * block_mask[:, None, :, None]
    block_sums = tree_sum(
        jnp.einsum(
            "bitk,btkr->bir", blocks, kr_masked, preferred_element_type=jnp.float32
        ).reshape(neuron_rows, rank_size),
        ("tm", "trial"),
    )
    raw_rows = apply_inverse(block_sums, inverse_neuron)
    own_rows = neuron_rows // (lax.axis_size("tm") * lax.axis_size("trial"))
    own_index = lax.axis_index("tm") * lax.axis_size("trial") + lax.axis_index("trial")
    own_columns = lax.dynamic_slice_in_dim(raw_rows, own_index * own_rows, own_rows, axis=1)
    gram_piece = tree_sum(
        jnp.dot(own_columns.T, raw_rows, precision=lax.Precision.HIGHEST), ("neuron",)
    )
    gram_sum = tree_gather(gram_piece, (("trial", 1), ("trial", 2), ("tm", 1)))
    neuron_local, gram_neuron = rescale(raw_rows, gram_sum, neuron_total)
    neuron_own = lax.dynamic_slice_in_dim(neuron_local, own_index * own_rows, own_rows, axis=0)
    neuron_blocks = neuron_local.reshape(block_count, block_rows, rank_size)
    time_total = time_rows * lax.axis_size("tm")

    def time_add_block(running, inputs):
        tensor_piece, mask_row, rows_a = inputs
        kr_ik = khatri_rao(rows_a, trial_factor) * mask_row[None, :, None]
        return (
            running
            + jnp.einsum("itk,ikr->tr", tensor_piece, kr_ik, preferred_element_type=jnp.float32),
            None,
        )

    running, unused = lax.scan(
        time_add_block,
        jnp.zeros((time_rows, rank_size), jnp.float32),
        (blocks, block_mask, neuron_blocks),
    )
    running, gram_neuron = lax.optimization_barrier((running, gram_neuron))
    half_sums = tree_sum(running, ("neuron", "trial"))
    inverse_time = normal_inverse(gram_neuron * start_trial)
    raw_rows = apply_inverse(half_sums, inverse_time)
    gram_sum = tree_sum(raw_gram(raw_rows), ("tm",))
    time_local, gram_time = rescale(raw_rows, gram_sum, time_total)
    trial_total = trial_rows * lax.axis_size("trial")

    def trial_add_block(running, inputs):
        tensor_piece, mask_row, rows_a = inputs
        kr_it = khatri_rao(rows_a, time_local)
        block_part = jnp.einsum(
            "itk,itr->kr", tensor_piece, kr_it, preferred_element_type=jnp.float32
        )
        return (running + block_part * mask_row.astype(jnp.float32)[:, None], None)

    running, unused = lax.scan(
        trial_add_block,
        jnp.zeros((trial_rows, rank_size), jnp.float32),
        (blocks, block_mask, neuron_blocks),
    )
    running, gram_time = lax.optimization_barrier((running, gram_time))
    quarter_sums = tree_sum(running, ("neuron", "tm"))
    inverse_trial = normal_inverse(gram_neuron * gram_time)
    raw_rows = apply_inverse(quarter_sums, inverse_trial)
    squares = tree_sum(jnp.sum(raw_rows * raw_rows, axis=0), ("trial",))
    scales = jnp.sqrt(squares / trial_total + EPSILON)
    trial_local = (raw_rows / scales[None, :]).astype(jnp.bfloat16)
    return (neuron_own, time_local, trial_local)


def solution(mesh):
    return jax.shard_map(
        on_device,
        mesh=mesh,
        in_specs=(
            P("neuron", "tm", "trial"),
            P("neuron", None),
            P("trial"),
            P("tm", None),
            P("trial", None),
        ),
        out_specs=(P(("neuron", "tm", "trial"), None), P("tm", None), P("trial", None)),
        check_vma=False,
    )
```

```python
import jax
import jax.numpy as jnp
from jax import lax
from jax.sharding import PartitionSpec as P

RIDGE = 0.1
EPSILON = 1e-06


def lower_inverse(lower_factor):
    size = lower_factor.shape[0]
    identity = jnp.eye(size, dtype=jnp.float32)
    return lax.linalg.triangular_solve(lower_factor, identity, left_side=True, lower=True)


def normal_inverse(gram_matrix):
    order_size = gram_matrix.shape[0]
    half = order_size // 2
    identity = jnp.eye(order_size, dtype=jnp.float32)
    scaled = gram_matrix / jnp.mean(jnp.diagonal(gram_matrix)) + RIDGE * identity
    scaled = (scaled + scaled.T) / 2
    lower_11 = lax.linalg.cholesky(scaled[:half, :half], symmetrize_input=False)
    inverse_11 = lower_inverse(lower_11)
    lower_21 = jnp.dot(scaled[half:, :half], inverse_11.T, precision=lax.Precision.HIGHEST)
    schur = scaled[half:, half:] - jnp.dot(
        lower_21, lower_21.T, precision=lax.Precision.HIGHEST
    )
    lower_22 = lax.linalg.cholesky(schur, symmetrize_input=False)
    inverse_22 = lower_inverse(lower_22)
    inverse_21 = -jnp.dot(
        jnp.dot(inverse_22, lower_21, precision=lax.Precision.HIGHEST),
        inverse_11,
        precision=lax.Precision.HIGHEST,
    )
    top = jnp.concatenate([inverse_11, jnp.zeros_like(inverse_11)], axis=1)
    bottom = jnp.concatenate([inverse_21, inverse_22], axis=1)
    return jnp.concatenate([top, bottom], axis=0)


def apply_inverse(partial_sums, inverse_factor):
    half = jnp.dot(partial_sums, inverse_factor.T, precision=lax.Precision.HIGHEST)
    return jnp.dot(half, inverse_factor, precision=lax.Precision.HIGHEST)


def raw_gram(raw_rows):
    return jnp.dot(raw_rows.T, raw_rows, precision=lax.Precision.HIGHEST)


def khatri_rao(left_rows, right_rows):
    return (
        left_rows.astype(jnp.float32)[:, None, :] * right_rows.astype(jnp.float32)[None, :, :]
    ).astype(jnp.bfloat16)


def rescale(raw_rows, gram_sum, total_rows):
    scales = jnp.sqrt(jnp.diagonal(gram_sum) / total_rows + EPSILON)
    factor = (raw_rows / scales[None, :]).astype(jnp.bfloat16)
    normed = gram_sum / (scales[:, None] * scales[None, :])
    return (factor, normed)


def block_mask_of(present_blocks, trial_day):
    day_count = present_blocks.shape[1]
    onehot = (trial_day[:, None] == jnp.arange(day_count, dtype=jnp.int32)[None, :]).astype(
        jnp.float32
    )
    return jnp.dot(present_blocks.astype(jnp.float32), onehot.T).astype(jnp.bfloat16)


def tree_sum(values, axes):
    for axis in axes:
        size = lax.axis_size(axis)
        stride = 1
        while stride < size:
            pairs = [(i, i ^ stride) for i in range(size)]
            values = values + lax.ppermute(values, axis, pairs)
            stride *= 2
    return values


def tree_gather(piece, steps):
    for axis, stride in steps:
        pairs = [(i, i ^ stride) for i in range(lax.axis_size(axis))]
        other = lax.ppermute(piece, axis, pairs)
        upper = (lax.axis_index(axis) // stride) % 2 == 1
        piece = jnp.where(
            upper,
            jnp.concatenate([other, piece], axis=0),
            jnp.concatenate([piece, other], axis=0),
        )
    return piece


def factor_gram(rows):
    return jnp.dot(rows.T, rows, preferred_element_type=jnp.float32)


def on_device(tensor, present_blocks, trial_day, time_factor, trial_factor):
    block_mask = block_mask_of(present_blocks, trial_day)
    block_count = present_blocks.shape[0]
    neuron_rows, time_rows, trial_rows = tensor.shape
    block_rows = neuron_rows // block_count
    blocks = tensor.reshape(block_count, block_rows, time_rows, trial_rows)
    rank_size = time_factor.shape[1]
    start_time = tree_sum(factor_gram(time_factor), ("tm",))
    start_trial = tree_sum(factor_gram(trial_factor), ("trial",))
    inverse_neuron = normal_inverse(start_time * start_trial)
    kr_tk = khatri_rao(time_factor, trial_factor)
    neuron_total = neuron_rows * lax.axis_size("neuron")
    kr_masked = kr_tk[None, :, :, :] * block_mask[:, None, :, None]
    block_sums = tree_sum(
        jnp.einsum(
            "bitk,btkr->bir", blocks, kr_masked, preferred_element_type=jnp.float32
        ).reshape(neuron_rows, rank_size),
        ("tm", "trial"),
    )
    raw_rows = apply_inverse(block_sums, inverse_neuron)
    own_rows = neuron_rows // (lax.axis_size("tm") * lax.axis_size("trial"))
    own_index = lax.axis_index("tm") * lax.axis_size("trial") + lax.axis_index("trial")
    own_columns = lax.dynamic_slice_in_dim(raw_rows, own_index * own_rows, own_rows, axis=1)
    gram_piece = tree_sum(
        jnp.dot(own_columns.T, raw_rows, precision=lax.Precision.HIGHEST), ("neuron",)
    )
    gram_sum = tree_gather(gram_piece, (("trial", 1), ("trial", 2), ("tm", 1)))
    neuron_local, gram_neuron = rescale(raw_rows, gram_sum, neuron_total)
    neuron_own = lax.dynamic_slice_in_dim(neuron_local, own_index * own_rows, own_rows, axis=0)
    neuron_blocks = neuron_local.reshape(block_count, block_rows, rank_size)
    time_total = time_rows * lax.axis_size("tm")

    def time_add_block(running, inputs):
        tensor_piece, mask_row, rows_a = inputs
        kr_ik = khatri_rao(rows_a, trial_factor) * mask_row[None, :, None]
        return (
            running
            + jnp.einsum("itk,ikr->tr", tensor_piece, kr_ik, preferred_element_type=jnp.float32),
            None,
        )

    running, unused = lax.scan(
        time_add_block,
        jnp.zeros((time_rows, rank_size), jnp.float32),
        (blocks, block_mask, neuron_blocks),
    )
    running, gram_neuron = lax.optimization_barrier((running, gram_neuron))
    half_sums = tree_sum(running, ("neuron", "trial"))
    inverse_time = normal_inverse(gram_neuron * start_trial)
    raw_rows = apply_inverse(half_sums, inverse_time)
    gram_sum = tree_sum(raw_gram(raw_rows), ("tm",))
    time_local, gram_time = rescale(raw_rows, gram_sum, time_total)
    trial_total = trial_rows * lax.axis_size("trial")

    def trial_add_block(running, inputs):
        tensor_piece, mask_row, rows_a = inputs
        kr_it = khatri_rao(rows_a, time_local)
        block_part = jnp.einsum(
            "itk,itr->kr", tensor_piece, kr_it, preferred_element_type=jnp.float32
        )
        return (running + block_part * mask_row.astype(jnp.float32)[:, None], None)

    running, unused = lax.scan(
        trial_add_block,
        jnp.zeros((trial_rows, rank_size), jnp.float32),
        (blocks, block_mask, neuron_blocks),
    )
    running, gram_time = lax.optimization_barrier((running, gram_time))
    quarter_sums = tree_sum(running, ("neuron", "tm"))
    inverse_trial = normal_inverse(gram_neuron * gram_time)
    raw_rows = apply_inverse(quarter_sums, inverse_trial)
    squares = tree_sum(jnp.sum(raw_rows * raw_rows, axis=0), ("trial",))
    scales = jnp.sqrt(squares / trial_total + EPSILON)
    trial_local = (raw_rows / scales[None, :]).astype(jnp.bfloat16)
    return (neuron_own, time_local, trial_local)


def solution(mesh):
    return jax.shard_map(
        on_device,
        mesh=mesh,
        in_specs=(
            P("neuron", "tm", "trial"),
            P("neuron", None),
            P("trial"),
            P("tm", None),
            P("trial", None),
        ),
        out_specs=(P(("neuron", "tm", "trial"), None), P("tm", None), P("trial", None)),
        check_vma=False,
    )
```

```python
import jax
import jax.numpy as jnp
from jax import lax
from jax.sharding import PartitionSpec as P

RIDGE = 0.1
EPSILON = 1e-06


def lower_inverse(lower_factor):
    size = lower_factor.shape[0]
    identity = jnp.eye(size, dtype=jnp.float32)
    return lax.linalg.triangular_solve(lower_factor, identity, left_side=True, lower=True)


def normal_inverse(gram_matrix):
    order_size = gram_matrix.shape[0]
    half = order_size // 2
    identity = jnp.eye(order_size, dtype=jnp.float32)
    scaled = gram_matrix / jnp.mean(jnp.diagonal(gram_matrix)) + RIDGE * identity
    scaled = (scaled + scaled.T) / 2
    lower_11 = lax.linalg.cholesky(scaled[:half, :half], symmetrize_input=False)
    inverse_11 = lower_inverse(lower_11)
    lower_21 = jnp.dot(scaled[half:, :half], inverse_11.T, precision=lax.Precision.HIGHEST)
    schur = scaled[half:, half:] - jnp.dot(
        lower_21, lower_21.T, precision=lax.Precision.HIGHEST
    )
    lower_22 = lax.linalg.cholesky(schur, symmetrize_input=False)
    inverse_22 = lower_inverse(lower_22)
    inverse_21 = -jnp.dot(
        jnp.dot(inverse_22, lower_21, precision=lax.Precision.HIGHEST),
        inverse_11,
        precision=lax.Precision.HIGHEST,
    )
    top = jnp.concatenate([inverse_11, jnp.zeros_like(inverse_11)], axis=1)
    bottom = jnp.concatenate([inverse_21, inverse_22], axis=1)
    return jnp.concatenate([top, bottom], axis=0)


def apply_inverse(partial_sums, inverse_factor):
    half = jnp.dot(partial_sums, inverse_factor.T, precision=lax.Precision.HIGHEST)
    return jnp.dot(half, inverse_factor, precision=lax.Precision.HIGHEST)


def raw_gram(raw_rows):
    return jnp.dot(raw_rows.T, raw_rows, precision=lax.Precision.HIGHEST)


def khatri_rao(left_rows, right_rows):
    return (
        left_rows.astype(jnp.float32)[:, None, :] * right_rows.astype(jnp.float32)[None, :, :]
    ).astype(jnp.bfloat16)


def rescale(raw_rows, gram_sum, total_rows):
    scales = jnp.sqrt(jnp.diagonal(gram_sum) / total_rows + EPSILON)
    factor = (raw_rows / scales[None, :]).astype(jnp.bfloat16)
    normed = gram_sum / (scales[:, None] * scales[None, :])
    return (factor, normed)


def block_mask_of(present_blocks, trial_day):
    day_count = present_blocks.shape[1]
    onehot = (trial_day[:, None] == jnp.arange(day_count, dtype=jnp.int32)[None, :]).astype(
        jnp.float32
    )
    return jnp.dot(present_blocks.astype(jnp.float32), onehot.T).astype(jnp.bfloat16)


def tree_sum(values, axes):
    for axis in axes:
        size = lax.axis_size(axis)
        stride = 1
        while stride < size:
            pairs = [(i, i ^ stride) for i in range(size)]
            values = values + lax.ppermute(values, axis, pairs)
            stride *= 2
    return values


def tree_gather(piece, steps):
    for axis, stride in steps:
        pairs = [(i, i ^ stride) for i in range(lax.axis_size(axis))]
        other = lax.ppermute(piece, axis, pairs)
        upper = (lax.axis_index(axis) // stride) % 2 == 1
        piece = jnp.where(
            upper,
            jnp.concatenate([other, piece], axis=0),
            jnp.concatenate([piece, other], axis=0),
        )
    return piece


def factor_gram(rows):
    return jnp.dot(rows.T, rows, preferred_element_type=jnp.float32)


def on_device(tensor, present_blocks, trial_day, time_factor, trial_factor):
    block_mask = block_mask_of(present_blocks, trial_day)
    block_count = present_blocks.shape[0]
    neuron_rows, time_rows, trial_rows = tensor.shape
    block_rows = neuron_rows // block_count
    blocks = tensor.reshape(block_count, block_rows, time_rows, trial_rows)
    rank_size = time_factor.shape[1]
    start_time = tree_sum(factor_gram(time_factor), ("tm",))
    start_trial = tree_sum(factor_gram(trial_factor), ("trial",))
    inverse_neuron = normal_inverse(start_time * start_trial)
    kr_tk = khatri_rao(time_factor, trial_factor)
    neuron_total = neuron_rows * lax.axis_size("neuron")
    kr_masked = kr_tk[None, :, :, :] * block_mask[:, None, :, None]
    block_sums = tree_sum(
        jnp.einsum(
            "bitk,btkr->bir", blocks, kr_masked, preferred_element_type=jnp.float32
        ).reshape(neuron_rows, rank_size),
        ("tm", "trial"),
    )
    raw_rows = apply_inverse(block_sums, inverse_neuron)
    own_rows = neuron_rows // (lax.axis_size("tm") * lax.axis_size("trial"))
    own_index = lax.axis_index("tm") * lax.axis_size("trial") + lax.axis_index("trial")
    own_columns = lax.dynamic_slice_in_dim(raw_rows, own_index * own_rows, own_rows, axis=1)
    gram_piece = tree_sum(
        jnp.dot(own_columns.T, raw_rows, precision=lax.Precision.HIGHEST), ("neuron",)
    )
    gram_sum = tree_gather(gram_piece, (("trial", 1), ("trial", 2), ("tm", 1)))
    neuron_local, gram_neuron = rescale(raw_rows, gram_sum, neuron_total)
    neuron_own = lax.dynamic_slice_in_dim(neuron_local, own_index * own_rows, own_rows, axis=0)
    neuron_blocks = neuron_local.reshape(block_count, block_rows, rank_size)
    time_total = time_rows * lax.axis_size("tm")

    def time_add_block(running, inputs):
        tensor_piece, mask_row, rows_a = inputs
        kr_ik = khatri_rao(rows_a, trial_factor) * mask_row[None, :, None]
        return (
            running
            + jnp.einsum("itk,ikr->tr", tensor_piece, kr_ik, preferred_element_type=jnp.float32),
            None,
        )

    running, unused = lax.scan(
        time_add_block,
        jnp.zeros((time_rows, rank_size), jnp.float32),
        (blocks, block_mask, neuron_blocks),
    )
    running, gram_neuron = lax.optimization_barrier((running, gram_neuron))
    half_sums = tree_sum(running, ("neuron", "trial"))
    inverse_time = normal_inverse(gram_neuron * start_trial)
    raw_rows = apply_inverse(half_sums, inverse_time)
    gram_sum = tree_sum(raw_gram(raw_rows), ("tm",))
    time_local, gram_time = rescale(raw_rows, gram_sum, time_total)
    trial_total = trial_rows * lax.axis_size("trial")

    blocks_kt = jnp.swapaxes(blocks, 2, 3)

    def trial_add_block(running, inputs):
        tensor_piece, mask_row, rows_a = inputs
        kr_it = khatri_rao(rows_a, time_local)
        block_part = jnp.einsum(
            "ikt,itr->kr", tensor_piece, kr_it, preferred_element_type=jnp.float32
        )
        return (running + block_part * mask_row.astype(jnp.float32)[:, None], None)

    running, unused = lax.scan(
        trial_add_block,
        jnp.zeros((trial_rows, rank_size), jnp.float32),
        (blocks_kt, block_mask, neuron_blocks),
    )
    running, gram_time = lax.optimization_barrier((running, gram_time))
    quarter_sums = tree_sum(running, ("neuron", "tm"))
    inverse_trial = normal_inverse(gram_neuron * gram_time)
    raw_rows = apply_inverse(quarter_sums, inverse_trial)
    squares = tree_sum(jnp.sum(raw_rows * raw_rows, axis=0), ("trial",))
    scales = jnp.sqrt(squares / trial_total + EPSILON)
    trial_local = (raw_rows / scales[None, :]).astype(jnp.bfloat16)
    return (neuron_own, time_local, trial_local)


def solution(mesh):
    return jax.shard_map(
        on_device,
        mesh=mesh,
        in_specs=(
            P("neuron", "tm", "trial"),
            P("neuron", None),
            P("trial"),
            P("tm", None),
            P("trial", None),
        ),
        out_specs=(P(("neuron", "tm", "trial"), None), P("tm", None), P("trial", None)),
        check_vma=False,
    )
```

```python
import jax
import jax.numpy as jnp
from jax import lax
from jax.experimental import pallas as pl
from jax.experimental.pallas import tpu as pltpu
from jax.sharding import PartitionSpec as P

RIDGE = 0.1
EPSILON = 1e-06


def lower_inverse(lower_factor):
    size = lower_factor.shape[0]
    identity = jnp.eye(size, dtype=jnp.float32)
    return lax.linalg.triangular_solve(lower_factor, identity, left_side=True, lower=True)


def normal_inverse(gram_matrix):
    order_size = gram_matrix.shape[0]
    half = order_size // 2
    identity = jnp.eye(order_size, dtype=jnp.float32)
    scaled = gram_matrix / jnp.mean(jnp.diagonal(gram_matrix)) + RIDGE * identity
    scaled = (scaled + scaled.T) / 2
    lower_11 = lax.linalg.cholesky(scaled[:half, :half], symmetrize_input=False)
    inverse_11 = lower_inverse(lower_11)
    lower_21 = jnp.dot(scaled[half:, :half], inverse_11.T, precision=lax.Precision.HIGHEST)
    schur = scaled[half:, half:] - jnp.dot(
        lower_21, lower_21.T, precision=lax.Precision.HIGHEST
    )
    lower_22 = lax.linalg.cholesky(schur, symmetrize_input=False)
    inverse_22 = lower_inverse(lower_22)
    inverse_21 = -jnp.dot(
        jnp.dot(inverse_22, lower_21, precision=lax.Precision.HIGHEST),
        inverse_11,
        precision=lax.Precision.HIGHEST,
    )
    top = jnp.concatenate([inverse_11, jnp.zeros_like(inverse_11)], axis=1)
    bottom = jnp.concatenate([inverse_21, inverse_22], axis=1)
    return jnp.concatenate([top, bottom], axis=0)


def apply_inverse(partial_sums, inverse_factor):
    half = jnp.dot(partial_sums, inverse_factor.T, precision=lax.Precision.HIGHEST)
    return jnp.dot(half, inverse_factor, precision=lax.Precision.HIGHEST)


def raw_gram(raw_rows):
    return jnp.dot(raw_rows.T, raw_rows, precision=lax.Precision.HIGHEST)


def khatri_rao(left_rows, right_rows):
    return (
        left_rows.astype(jnp.float32)[:, None, :] * right_rows.astype(jnp.float32)[None, :, :]
    ).astype(jnp.bfloat16)


def rescale(raw_rows, gram_sum, total_rows):
    scales = jnp.sqrt(jnp.diagonal(gram_sum) / total_rows + EPSILON)
    factor = (raw_rows / scales[None, :]).astype(jnp.bfloat16)
    normed = gram_sum / (scales[:, None] * scales[None, :])
    return (factor, normed)


def block_mask_of(present_blocks, trial_day):
    day_count = present_blocks.shape[1]
    onehot = (trial_day[:, None] == jnp.arange(day_count, dtype=jnp.int32)[None, :]).astype(
        jnp.float32
    )
    return jnp.dot(present_blocks.astype(jnp.float32), onehot.T).astype(jnp.bfloat16)


def tree_sum(values, axes):
    for axis in axes:
        size = lax.axis_size(axis)
        stride = 1
        while stride < size:
            pairs = [(i, i ^ stride) for i in range(size)]
            values = values + lax.ppermute(values, axis, pairs)
            stride *= 2
    return values


def tree_gather(piece, steps):
    for axis, stride in steps:
        pairs = [(i, i ^ stride) for i in range(lax.axis_size(axis))]
        other = lax.ppermute(piece, axis, pairs)
        upper = (lax.axis_index(axis) // stride) % 2 == 1
        piece = jnp.where(
            upper,
            jnp.concatenate([other, piece], axis=0),
            jnp.concatenate([piece, other], axis=0),
        )
    return piece


def block_matmul_kernel(lhs_ref, rhs_ref, out_ref, acc_ref):
    @pl.when(pl.program_id(1) == 0)
    def _():
        acc_ref[...] = jnp.zeros_like(acc_ref)

    acc_ref[...] += jnp.dot(lhs_ref[...], rhs_ref[0], preferred_element_type=jnp.float32)

    @pl.when(pl.program_id(1) == pl.num_programs(1) - 1)
    def _():
        out_ref[...] = acc_ref[...]


def block_matmul(lhs, rhs, chunk=2048):
    rows, depth = lhs.shape
    block_count, _, width = rhs.shape
    block_rows = rows // block_count
    return pl.pallas_call(
        block_matmul_kernel,
        grid=(block_count, depth // chunk),
        in_specs=[
            pl.BlockSpec((block_rows, chunk), lambda b, c: (b, c)),
            pl.BlockSpec((1, chunk, width), lambda b, c: (b, c, 0)),
        ],
        out_specs=pl.BlockSpec((block_rows, width), lambda b, c: (b, 0)),
        out_shape=jax.ShapeDtypeStruct((rows, width), jnp.float32),
        scratch_shapes=[pltpu.VMEM((block_rows, width), jnp.float32)],
    )(lhs, rhs)


def factor_gram(rows):
    return jnp.dot(rows.T, rows, preferred_element_type=jnp.float32)


def on_device(tensor, present_blocks, trial_day, time_factor, trial_factor):
    block_mask = block_mask_of(present_blocks, trial_day)
    block_count = present_blocks.shape[0]
    neuron_rows, time_rows, trial_rows = tensor.shape
    block_rows = neuron_rows // block_count
    blocks = tensor.reshape(block_count, block_rows, time_rows, trial_rows)
    rank_size = time_factor.shape[1]
    start_time = tree_sum(factor_gram(time_factor), ("tm",))
    start_trial = tree_sum(factor_gram(trial_factor), ("trial",))
    inverse_neuron = normal_inverse(start_time * start_trial)
    kr_tk = khatri_rao(time_factor, trial_factor)
    neuron_total = neuron_rows * lax.axis_size("neuron")
    kr_masked = kr_tk[None, :, :, :] * block_mask[:, None, :, None]
    block_sums = tree_sum(
        block_matmul(
            tensor.reshape(neuron_rows, time_rows * trial_rows),
            kr_masked.reshape(block_count, time_rows * trial_rows, rank_size),
        ),
        ("tm", "trial"),
    )
    raw_rows = apply_inverse(block_sums, inverse_neuron)
    own_rows = neuron_rows // (lax.axis_size("tm") * lax.axis_size("trial"))
    own_index = lax.axis_index("tm") * lax.axis_size("trial") + lax.axis_index("trial")
    own_columns = lax.dynamic_slice_in_dim(raw_rows, own_index * own_rows, own_rows, axis=1)
    gram_piece = tree_sum(
        jnp.dot(own_columns.T, raw_rows, precision=lax.Precision.HIGHEST), ("neuron",)
    )
    gram_sum = tree_gather(gram_piece, (("trial", 1), ("trial", 2), ("tm", 1)))
    neuron_local, gram_neuron = rescale(raw_rows, gram_sum, neuron_total)
    neuron_own = lax.dynamic_slice_in_dim(neuron_local, own_index * own_rows, own_rows, axis=0)
    neuron_blocks = neuron_local.reshape(block_count, block_rows, rank_size)
    time_total = time_rows * lax.axis_size("tm")

    def time_add_block(running, inputs):
        tensor_piece, mask_row, rows_a = inputs
        kr_ik = khatri_rao(rows_a, trial_factor) * mask_row[None, :, None]
        return (
            running
            + jnp.einsum("itk,ikr->tr", tensor_piece, kr_ik, preferred_element_type=jnp.float32),
            None,
        )

    running, unused = lax.scan(
        time_add_block,
        jnp.zeros((time_rows, rank_size), jnp.float32),
        (blocks, block_mask, neuron_blocks),
    )
    running, gram_neuron = lax.optimization_barrier((running, gram_neuron))
    half_sums = tree_sum(running, ("neuron", "trial"))
    inverse_time = normal_inverse(gram_neuron * start_trial)
    raw_rows = apply_inverse(half_sums, inverse_time)
    gram_sum = tree_sum(raw_gram(raw_rows), ("tm",))
    time_local, gram_time = rescale(raw_rows, gram_sum, time_total)
    trial_total = trial_rows * lax.axis_size("trial")

    blocks_kt = jnp.swapaxes(blocks, 2, 3)

    def trial_add_block(running, inputs):
        tensor_piece, mask_row, rows_a = inputs
        kr_it = khatri_rao(rows_a, time_local)
        block_part = jnp.einsum(
            "ikt,itr->kr", tensor_piece, kr_it, preferred_element_type=jnp.float32
        )
        return (running + block_part * mask_row.astype(jnp.float32)[:, None], None)

    running, unused = lax.scan(
        trial_add_block,
        jnp.zeros((trial_rows, rank_size), jnp.float32),
        (blocks_kt, block_mask, neuron_blocks),
    )
    running, gram_time = lax.optimization_barrier((running, gram_time))
    quarter_sums = tree_sum(running, ("neuron", "tm"))
    inverse_trial = normal_inverse(gram_neuron * gram_time)
    raw_rows = apply_inverse(quarter_sums, inverse_trial)
    squares = tree_sum(jnp.sum(raw_rows * raw_rows, axis=0), ("trial",))
    scales = jnp.sqrt(squares / trial_total + EPSILON)
    trial_local = (raw_rows / scales[None, :]).astype(jnp.bfloat16)
    return (neuron_own, time_local, trial_local)


def solution(mesh):
    return jax.shard_map(
        on_device,
        mesh=mesh,
        in_specs=(
            P("neuron", "tm", "trial"),
            P("neuron", None),
            P("trial"),
            P("tm", None),
            P("trial", None),
        ),
        out_specs=(P(("neuron", "tm", "trial"), None), P("tm", None), P("trial", None)),
        check_vma=False,
    )
```

```python
import jax
import jax.numpy as jnp
from jax import lax
from jax.experimental import pallas as pl
from jax.experimental.pallas import tpu as pltpu
from jax.sharding import PartitionSpec as P

RIDGE = 0.1
EPSILON = 1e-06


def lower_inverse(lower_factor):
    size = lower_factor.shape[0]
    identity = jnp.eye(size, dtype=jnp.float32)
    return lax.linalg.triangular_solve(lower_factor, identity, left_side=True, lower=True)


def normal_inverse(gram_matrix):
    order_size = gram_matrix.shape[0]
    half = order_size // 2
    identity = jnp.eye(order_size, dtype=jnp.float32)
    scaled = gram_matrix / jnp.mean(jnp.diagonal(gram_matrix)) + RIDGE * identity
    scaled = (scaled + scaled.T) / 2
    lower_11 = lax.linalg.cholesky(scaled[:half, :half], symmetrize_input=False)
    inverse_11 = lower_inverse(lower_11)
    lower_21 = jnp.dot(scaled[half:, :half], inverse_11.T, precision=lax.Precision.HIGHEST)
    schur = scaled[half:, half:] - jnp.dot(
        lower_21, lower_21.T, precision=lax.Precision.HIGHEST
    )
    lower_22 = lax.linalg.cholesky(schur, symmetrize_input=False)
    inverse_22 = lower_inverse(lower_22)
    inverse_21 = -jnp.dot(
        jnp.dot(inverse_22, lower_21, precision=lax.Precision.HIGHEST),
        inverse_11,
        precision=lax.Precision.HIGHEST,
    )
    top = jnp.concatenate([inverse_11, jnp.zeros_like(inverse_11)], axis=1)
    bottom = jnp.concatenate([inverse_21, inverse_22], axis=1)
    return jnp.concatenate([top, bottom], axis=0)


def apply_inverse(partial_sums, inverse_factor):
    half = jnp.dot(partial_sums, inverse_factor.T, precision=lax.Precision.HIGHEST)
    return jnp.dot(half, inverse_factor, precision=lax.Precision.HIGHEST)


def raw_gram(raw_rows):
    return jnp.dot(raw_rows.T, raw_rows, precision=lax.Precision.HIGHEST)


def khatri_rao(left_rows, right_rows):
    return (
        left_rows.astype(jnp.float32)[:, None, :] * right_rows.astype(jnp.float32)[None, :, :]
    ).astype(jnp.bfloat16)


def rescale(raw_rows, gram_sum, total_rows):
    scales = jnp.sqrt(jnp.diagonal(gram_sum) / total_rows + EPSILON)
    factor = (raw_rows / scales[None, :]).astype(jnp.bfloat16)
    normed = gram_sum / (scales[:, None] * scales[None, :])
    return (factor, normed)


def block_mask_of(present_blocks, trial_day):
    day_count = present_blocks.shape[1]
    onehot = (trial_day[:, None] == jnp.arange(day_count, dtype=jnp.int32)[None, :]).astype(
        jnp.float32
    )
    return jnp.dot(present_blocks.astype(jnp.float32), onehot.T).astype(jnp.bfloat16)


def tree_sum(values, axes):
    for axis in axes:
        size = lax.axis_size(axis)
        stride = 1
        while stride < size:
            pairs = [(i, i ^ stride) for i in range(size)]
            values = values + lax.ppermute(values, axis, pairs)
            stride *= 2
    return values


def tree_gather(piece, steps):
    for axis, stride in steps:
        pairs = [(i, i ^ stride) for i in range(lax.axis_size(axis))]
        other = lax.ppermute(piece, axis, pairs)
        upper = (lax.axis_index(axis) // stride) % 2 == 1
        piece = jnp.where(
            upper,
            jnp.concatenate([other, piece], axis=0),
            jnp.concatenate([piece, other], axis=0),
        )
    return piece


def neuron_kernel(lhs_ref, time_ref, trial_ref, out_ref, acc_ref):
    @pl.when(pl.program_id(1) == 0)
    def _():
        acc_ref[...] = jnp.zeros_like(acc_ref)

    trial_rows = trial_ref[0].astype(jnp.float32)
    width = trial_rows.shape[0]
    total = acc_ref[...]
    for j in range(time_ref.shape[0]):
        kr = (time_ref[j:j + 1, :].astype(jnp.float32) * trial_rows).astype(jnp.bfloat16)
        total += jnp.dot(
            lhs_ref[:, j * width:(j + 1) * width], kr, preferred_element_type=jnp.float32
        )
    acc_ref[...] = total

    @pl.when(pl.program_id(1) == pl.num_programs(1) - 1)
    def _():
        out_ref[...] = acc_ref[...]


def neuron_mttkrp(tensor, time_factor, trial_masked, time_chunk=16):
    rows, time_rows, trial_rows = tensor.shape
    block_count, _, rank_size = trial_masked.shape
    block_rows = rows // block_count
    return pl.pallas_call(
        neuron_kernel,
        grid=(block_count, time_rows // time_chunk),
        in_specs=[
            pl.BlockSpec((block_rows, time_chunk * trial_rows), lambda b, c: (b, c)),
            pl.BlockSpec((time_chunk, rank_size), lambda b, c: (c, 0)),
            pl.BlockSpec((1, trial_rows, rank_size), lambda b, c: (b, 0, 0)),
        ],
        out_specs=pl.BlockSpec((block_rows, rank_size), lambda b, c: (b, 0)),
        out_shape=jax.ShapeDtypeStruct((rows, rank_size), jnp.float32),
        scratch_shapes=[pltpu.VMEM((block_rows, rank_size), jnp.float32)],
    )(tensor.reshape(rows, time_rows * trial_rows), time_factor, trial_masked)


def factor_gram(rows):
    return jnp.dot(rows.T, rows, preferred_element_type=jnp.float32)


def on_device(tensor, present_blocks, trial_day, time_factor, trial_factor):
    block_mask = block_mask_of(present_blocks, trial_day)
    block_count = present_blocks.shape[0]
    neuron_rows, time_rows, trial_rows = tensor.shape
    block_rows = neuron_rows // block_count
    blocks = tensor.reshape(block_count, block_rows, time_rows, trial_rows)
    rank_size = time_factor.shape[1]
    start_time = tree_sum(factor_gram(time_factor), ("tm",))
    start_trial = tree_sum(factor_gram(trial_factor), ("trial",))
    inverse_neuron = normal_inverse(start_time * start_trial)
    kr_tk = khatri_rao(time_factor, trial_factor)
    neuron_total = neuron_rows * lax.axis_size("neuron")
    trial_masked = trial_factor[None, :, :] * block_mask[:, :, None]
    block_sums = tree_sum(neuron_mttkrp(tensor, time_factor, trial_masked), ("tm", "trial"))
    raw_rows = apply_inverse(block_sums, inverse_neuron)
    own_rows = neuron_rows // (lax.axis_size("tm") * lax.axis_size("trial"))
    own_index = lax.axis_index("tm") * lax.axis_size("trial") + lax.axis_index("trial")
    own_columns = lax.dynamic_slice_in_dim(raw_rows, own_index * own_rows, own_rows, axis=1)
    gram_piece = tree_sum(
        jnp.dot(own_columns.T, raw_rows, precision=lax.Precision.HIGHEST), ("neuron",)
    )
    gram_sum = tree_gather(gram_piece, (("trial", 1), ("trial", 2), ("tm", 1)))
    neuron_local, gram_neuron = rescale(raw_rows, gram_sum, neuron_total)
    neuron_own = lax.dynamic_slice_in_dim(neuron_local, own_index * own_rows, own_rows, axis=0)
    neuron_blocks = neuron_local.reshape(block_count, block_rows, rank_size)
    time_total = time_rows * lax.axis_size("tm")

    def time_add_block(running, inputs):
        tensor_piece, mask_row, rows_a = inputs
        kr_ik = khatri_rao(rows_a, trial_factor) * mask_row[None, :, None]
        return (
            running
            + jnp.einsum("itk,ikr->tr", tensor_piece, kr_ik, preferred_element_type=jnp.float32),
            None,
        )

    running, unused = lax.scan(
        time_add_block,
        jnp.zeros((time_rows, rank_size), jnp.float32),
        (blocks, block_mask, neuron_blocks),
    )
    running, gram_neuron = lax.optimization_barrier((running, gram_neuron))
    half_sums = tree_sum(running, ("neuron", "trial"))
    inverse_time = normal_inverse(gram_neuron * start_trial)
    raw_rows = apply_inverse(half_sums, inverse_time)
    gram_sum = tree_sum(raw_gram(raw_rows), ("tm",))
    time_local, gram_time = rescale(raw_rows, gram_sum, time_total)
    trial_total = trial_rows * lax.axis_size("trial")

    blocks_kt = jnp.swapaxes(blocks, 2, 3)

    def trial_add_block(running, inputs):
        tensor_piece, mask_row, rows_a = inputs
        kr_it = khatri_rao(rows_a, time_local)
        block_part = jnp.einsum(
            "ikt,itr->kr", tensor_piece, kr_it, preferred_element_type=jnp.float32
        )
        return (running + block_part * mask_row.astype(jnp.float32)[:, None], None)

    running, unused = lax.scan(
        trial_add_block,
        jnp.zeros((trial_rows, rank_size), jnp.float32),
        (blocks_kt, block_mask, neuron_blocks),
    )
    running, gram_time = lax.optimization_barrier((running, gram_time))
    quarter_sums = tree_sum(running, ("neuron", "tm"))
    inverse_trial = normal_inverse(gram_neuron * gram_time)
    raw_rows = apply_inverse(quarter_sums, inverse_trial)
    squares = tree_sum(jnp.sum(raw_rows * raw_rows, axis=0), ("trial",))
    scales = jnp.sqrt(squares / trial_total + EPSILON)
    trial_local = (raw_rows / scales[None, :]).astype(jnp.bfloat16)
    return (neuron_own, time_local, trial_local)


def solution(mesh):
    return jax.shard_map(
        on_device,
        mesh=mesh,
        in_specs=(
            P("neuron", "tm", "trial"),
            P("neuron", None),
            P("trial"),
            P("tm", None),
            P("trial", None),
        ),
        out_specs=(P(("neuron", "tm", "trial"), None), P("tm", None), P("trial", None)),
        check_vma=False,
    )
```

```python
import jax
import jax.numpy as jnp
from jax import lax
from jax.experimental import pallas as pl
from jax.experimental.pallas import tpu as pltpu
from jax.sharding import PartitionSpec as P

RIDGE = 0.1
EPSILON = 1e-06


def lower_inverse(lower_factor):
    size = lower_factor.shape[0]
    identity = jnp.eye(size, dtype=jnp.float32)
    return lax.linalg.triangular_solve(lower_factor, identity, left_side=True, lower=True)


def normal_inverse(gram_matrix):
    order_size = gram_matrix.shape[0]
    half = order_size // 2
    identity = jnp.eye(order_size, dtype=jnp.float32)
    scaled = gram_matrix / jnp.mean(jnp.diagonal(gram_matrix)) + RIDGE * identity
    scaled = (scaled + scaled.T) / 2
    lower_11 = lax.linalg.cholesky(scaled[:half, :half], symmetrize_input=False)
    inverse_11 = lower_inverse(lower_11)
    lower_21 = jnp.dot(scaled[half:, :half], inverse_11.T, precision=lax.Precision.HIGHEST)
    schur = scaled[half:, half:] - jnp.dot(
        lower_21, lower_21.T, precision=lax.Precision.HIGHEST
    )
    lower_22 = lax.linalg.cholesky(schur, symmetrize_input=False)
    inverse_22 = lower_inverse(lower_22)
    inverse_21 = -jnp.dot(
        jnp.dot(inverse_22, lower_21, precision=lax.Precision.HIGHEST),
        inverse_11,
        precision=lax.Precision.HIGHEST,
    )
    top = jnp.concatenate([inverse_11, jnp.zeros_like(inverse_11)], axis=1)
    bottom = jnp.concatenate([inverse_21, inverse_22], axis=1)
    return jnp.concatenate([top, bottom], axis=0)


def apply_inverse(partial_sums, inverse_factor):
    half = jnp.dot(partial_sums, inverse_factor.T, precision=lax.Precision.HIGHEST)
    return jnp.dot(half, inverse_factor, precision=lax.Precision.HIGHEST)


def raw_gram(raw_rows):
    return jnp.dot(raw_rows.T, raw_rows, precision=lax.Precision.HIGHEST)


def khatri_rao(left_rows, right_rows):
    return (
        left_rows.astype(jnp.float32)[:, None, :] * right_rows.astype(jnp.float32)[None, :, :]
    ).astype(jnp.bfloat16)


def rescale(raw_rows, gram_sum, total_rows):
    scales = jnp.sqrt(jnp.diagonal(gram_sum) / total_rows + EPSILON)
    factor = (raw_rows / scales[None, :]).astype(jnp.bfloat16)
    normed = gram_sum / (scales[:, None] * scales[None, :])
    return (factor, normed)


def block_mask_of(present_blocks, trial_day):
    day_count = present_blocks.shape[1]
    onehot = (trial_day[:, None] == jnp.arange(day_count, dtype=jnp.int32)[None, :]).astype(
        jnp.float32
    )
    return jnp.dot(present_blocks.astype(jnp.float32), onehot.T).astype(jnp.bfloat16)


def tree_sum(values, axes):
    for axis in axes:
        size = lax.axis_size(axis)
        stride = 1
        while stride < size:
            pairs = [(i, i ^ stride) for i in range(size)]
            values = values + lax.ppermute(values, axis, pairs)
            stride *= 2
    return values


def tree_gather(piece, steps):
    for axis, stride in steps:
        pairs = [(i, i ^ stride) for i in range(lax.axis_size(axis))]
        other = lax.ppermute(piece, axis, pairs)
        upper = (lax.axis_index(axis) // stride) % 2 == 1
        piece = jnp.where(
            upper,
            jnp.concatenate([other, piece], axis=0),
            jnp.concatenate([piece, other], axis=0),
        )
    return piece


def neuron_kernel(lhs_ref, time_ref, trial_ref, out_ref, acc_ref):
    @pl.when(pl.program_id(1) == 0)
    def _():
        acc_ref[...] = jnp.zeros_like(acc_ref)

    trial_rows = trial_ref[0].astype(jnp.float32)
    total = acc_ref[...]
    for j in range(time_ref.shape[0]):
        kr = (time_ref[j:j + 1, :].astype(jnp.float32) * trial_rows).astype(jnp.bfloat16)
        total += jnp.dot(lhs_ref[:, j, :], kr, preferred_element_type=jnp.float32)
    acc_ref[...] = total

    @pl.when(pl.program_id(1) == pl.num_programs(1) - 1)
    def _():
        out_ref[...] = acc_ref[...]


def neuron_mttkrp(tensor, time_factor, trial_masked, time_chunk=16):
    rows, time_rows, trial_rows = tensor.shape
    block_count, _, rank_size = trial_masked.shape
    block_rows = rows // block_count
    return pl.pallas_call(
        neuron_kernel,
        grid=(block_count, time_rows // time_chunk),
        in_specs=[
            pl.BlockSpec((block_rows, time_chunk, trial_rows), lambda b, c: (b, c, 0)),
            pl.BlockSpec((time_chunk, rank_size), lambda b, c: (c, 0)),
            pl.BlockSpec((1, trial_rows, rank_size), lambda b, c: (b, 0, 0)),
        ],
        out_specs=pl.BlockSpec((block_rows, rank_size), lambda b, c: (b, 0)),
        out_shape=jax.ShapeDtypeStruct((rows, rank_size), jnp.float32),
        scratch_shapes=[pltpu.VMEM((block_rows, rank_size), jnp.float32)],
    )(tensor, time_factor, trial_masked)


def factor_gram(rows):
    return jnp.dot(rows.T, rows, preferred_element_type=jnp.float32)


def on_device(tensor, present_blocks, trial_day, time_factor, trial_factor):
    block_mask = block_mask_of(present_blocks, trial_day)
    block_count = present_blocks.shape[0]
    neuron_rows, time_rows, trial_rows = tensor.shape
    block_rows = neuron_rows // block_count
    blocks = tensor.reshape(block_count, block_rows, time_rows, trial_rows)
    rank_size = time_factor.shape[1]
    start_time = tree_sum(factor_gram(time_factor), ("tm",))
    start_trial = tree_sum(factor_gram(trial_factor), ("trial",))
    inverse_neuron = normal_inverse(start_time * start_trial)
    kr_tk = khatri_rao(time_factor, trial_factor)
    neuron_total = neuron_rows * lax.axis_size("neuron")
    trial_masked = trial_factor[None, :, :] * block_mask[:, :, None]
    block_sums = tree_sum(neuron_mttkrp(tensor, time_factor, trial_masked), ("tm", "trial"))
    raw_rows = apply_inverse(block_sums, inverse_neuron)
    own_rows = neuron_rows // (lax.axis_size("tm") * lax.axis_size("trial"))
    own_index = lax.axis_index("tm") * lax.axis_size("trial") + lax.axis_index("trial")
    own_columns = lax.dynamic_slice_in_dim(raw_rows, own_index * own_rows, own_rows, axis=1)
    gram_piece = tree_sum(
        jnp.dot(own_columns.T, raw_rows, precision=lax.Precision.HIGHEST), ("neuron",)
    )
    gram_sum = tree_gather(gram_piece, (("trial", 1), ("trial", 2), ("tm", 1)))
    neuron_local, gram_neuron = rescale(raw_rows, gram_sum, neuron_total)
    neuron_own = lax.dynamic_slice_in_dim(neuron_local, own_index * own_rows, own_rows, axis=0)
    neuron_blocks = neuron_local.reshape(block_count, block_rows, rank_size)
    time_total = time_rows * lax.axis_size("tm")

    def time_add_block(running, inputs):
        tensor_piece, mask_row, rows_a = inputs
        kr_ik = khatri_rao(rows_a, trial_factor) * mask_row[None, :, None]
        return (
            running
            + jnp.einsum("itk,ikr->tr", tensor_piece, kr_ik, preferred_element_type=jnp.float32),
            None,
        )

    running, unused = lax.scan(
        time_add_block,
        jnp.zeros((time_rows, rank_size), jnp.float32),
        (blocks, block_mask, neuron_blocks),
    )
    running, gram_neuron = lax.optimization_barrier((running, gram_neuron))
    half_sums = tree_sum(running, ("neuron", "trial"))
    inverse_time = normal_inverse(gram_neuron * start_trial)
    raw_rows = apply_inverse(half_sums, inverse_time)
    gram_sum = tree_sum(raw_gram(raw_rows), ("tm",))
    time_local, gram_time = rescale(raw_rows, gram_sum, time_total)
    trial_total = trial_rows * lax.axis_size("trial")

    blocks_kt = jnp.swapaxes(blocks, 2, 3)

    def trial_add_block(running, inputs):
        tensor_piece, mask_row, rows_a = inputs
        kr_it = khatri_rao(rows_a, time_local)
        block_part = jnp.einsum(
            "ikt,itr->kr", tensor_piece, kr_it, preferred_element_type=jnp.float32
        )
        return (running + block_part * mask_row.astype(jnp.float32)[:, None], None)

    running, unused = lax.scan(
        trial_add_block,
        jnp.zeros((trial_rows, rank_size), jnp.float32),
        (blocks_kt, block_mask, neuron_blocks),
    )
    running, gram_time = lax.optimization_barrier((running, gram_time))
    quarter_sums = tree_sum(running, ("neuron", "tm"))
    inverse_trial = normal_inverse(gram_neuron * gram_time)
    raw_rows = apply_inverse(quarter_sums, inverse_trial)
    squares = tree_sum(jnp.sum(raw_rows * raw_rows, axis=0), ("trial",))
    scales = jnp.sqrt(squares / trial_total + EPSILON)
    trial_local = (raw_rows / scales[None, :]).astype(jnp.bfloat16)
    return (neuron_own, time_local, trial_local)


def solution(mesh):
    return jax.shard_map(
        on_device,
        mesh=mesh,
        in_specs=(
            P("neuron", "tm", "trial"),
            P("neuron", None),
            P("trial"),
            P("tm", None),
            P("trial", None),
        ),
        out_specs=(P(("neuron", "tm", "trial"), None), P("tm", None), P("trial", None)),
        check_vma=False,
    )
```
